512 devices in a mesh: seq: 128 (over x, z, y_hi), batch: 4 (over y_lo, core).
Axes of the slice: x: 4, y: 4 (y_hi: 2, y_lo: 2; y = y_hi * 2 + y_lo), z: 16, core: 2. Of those that a mesh axis runs over, the one named last changes fastest.
Arguments:
- inputs: bfloat16 [4, 128, 16384], P('batch', None, 'seq'), may hold values from -6 to 6
- out_grad: bfloat16 [4, 128, 16384], P('batch', None, 'seq'), may hold values from -0.046875 to 0.046875
- filters: float32 [128, 16384], P(None, 'seq'), may hold values from -6 to 6
Outputs:
- in_grad: bfloat16 [4, 128, 16384], P('batch', None, 'seq')
- filter_grad: float32 [128, 16384], P(None, 'seq')
The draws below stay inside these ranges and needn't reach their ends.
All inputs are finite; a program needn't handle non-finite values.
Results may differ from the reference program's by a relative error of at most 0.0025.
Values sent between devices are 32-bit elements; how exact they have to be, the bound alone decides.
No kernel may reach another device: no remote copies, remote signals or barrier semaphores. Data moves between devices by JAX's collectives and lax.ppermute only.
A program may use at most 64 MiB of HBM per device.

```python
import jax
import jax.numpy as jnp
from jax import lax

C = 128
LEN = 16384
SEQS = 4


def levels(stream_key, shape, split, smallest, high):
    gain, own = 1.0, jax.random.fold_in(stream_key, 6)
    for axis_at, parts in split:
        heights = jnp.exp(jax.random.uniform(jax.random.fold_in(own, axis_at), (parts,), jnp.float32, smallest / len(split), high / len(split)))
        gain = gain * jnp.repeat(heights, shape[axis_at] // parts).reshape([-1 if axis == axis_at else 1 for axis in range(len(shape))])
    return gain


def scatter_about(key, shape, deviation, limit, shards=(), kind=jnp.bfloat16):
    result = jax.random.normal(key, shape, jnp.float32) * deviation
    if len(shards) > 0:
        result = levels(key, shape, shards, -0.22, 0.18) * result
    return jnp.clip(result, min=-limit, max=limit).astype(kind)


def setup_inputs(seed: int = 0) -> dict:
    key_of = jax.random.split(jax.random.key(seed), 4)
    return {
        "inputs": scatter_about(key_of[0], (SEQS, C, LEN), 1.0, 6.0, ((0, 4), (2, 128))),
        "out_grad": scatter_about(key_of[1], (SEQS, C, LEN), LEN ** -0.5, 0.046875, ((0, 4), (2, 128))),
        "filters": scatter_about(key_of[2], (C, LEN), 1.0, 6.0, ((1, 128),), jnp.float32),
    }


def reference(inputs, out_grad, filters):
    fft_size = 2 * LEN
    spectrum_h = jnp.fft.rfft(filters.astype(jnp.float32), n=fft_size, axis=-1)

    def one_sequence(seq_pair):
        signal, cotangent = seq_pair
        spectrum_x = jnp.fft.rfft(signal.astype(jnp.float32), n=fft_size, axis=-1)
        spectrum_d = jnp.fft.rfft(cotangent.astype(jnp.float32), n=fft_size, axis=-1)
        grad_x = jnp.fft.irfft(jnp.conj(spectrum_h) * spectrum_d, n=fft_size, axis=-1)[:, :LEN]
        grad_h = jnp.fft.irfft(jnp.conj(spectrum_x) * spectrum_d, n=fft_size, axis=-1)[:, :LEN]
        return grad_x.astype(jnp.bfloat16), grad_h.astype(jnp.float32)

    grads_x, grads_h = lax.map(one_sequence, (inputs, out_grad))
    return grads_x, jnp.sum(grads_h, axis=0)
```

```python
import numpy as np

import jax
import jax.numpy as jnp
from jax import lax
from jax.sharding import PartitionSpec as P


def contract(pattern, operand, weights):
    return jnp.einsum(
        pattern,
        operand,
        weights,
        precision=lax.Precision.HIGHEST,
        preferred_element_type=jnp.float32,
    )


def freq_pairs(seq_count):
    low = np.arange(seq_count)
    second = np.where(low == 0, seq_count, 2 * seq_count - low)
    return np.stack([low, second], axis=1)


def tables(seq_count, total_len):
    pairs = freq_pairs(seq_count)
    k1 = pairs.reshape(-1)
    index = np.arange(seq_count)
    theta1 = 2.0 * np.pi * np.outer(index, k1) / (2 * seq_count)
    forward_p = np.concatenate([np.cos(theta1), np.sin(theta1)], axis=1)
    theta2 = 2.0 * np.pi * np.outer(index, index) / seq_count
    local = np.concatenate([np.cos(theta2), np.sin(theta2)], axis=1)
    k1_sr = pairs.T.reshape(-1)
    theta3 = 2.0 * np.pi * np.outer(k1_sr, index) / (2 * seq_count)
    inverse_p = np.concatenate([np.cos(theta3), np.sin(theta3)], axis=1) / total_len
    as32 = lambda a: jnp.asarray(a.astype(np.float32))
    return as32(forward_p), as32(local), as32(inverse_p), pairs.astype(np.int32)


def turn(real_part, imag_part, angle, orient):
    cosine = jnp.cos(angle)
    sine = jnp.sin(angle)
    return (
        real_part * cosine - orient * imag_part * sine,
        imag_part * cosine + orient * real_part * sine,
    )


def body(inputs, out_grad, filters):
    seq_count = lax.axis_size("seq")
    batch_count = lax.axis_size("batch")
    me = lax.axis_index("seq")
    mine = lax.axis_index("batch")
    channels = inputs.shape[1]
    length_dev = inputs.shape[2]
    assert length_dev == seq_count
    group = channels // batch_count
    sub = group // batch_count
    assert group * batch_count == channels and sub * batch_count == group
    total_len = 2 * seq_count * length_dev
    forward_p, local, inverse_p, pairs = tables(seq_count, total_len)
    f32 = jnp.float32

    signal = inputs[0].astype(f32).reshape(batch_count, group, length_dev)
    cotangent = out_grad[0].astype(f32).reshape(batch_count, group, length_dev)
    filt = lax.dynamic_index_in_dim(
        filters.reshape(batch_count, batch_count, sub, length_dev), mine, axis=1, keepdims=False
    )
    send = jnp.concatenate([signal, cotangent, filt], axis=1).transpose(2, 0, 1)
    width = 2 * group + sub
    send = send.reshape(seq_count * batch_count, width)
    recv = lax.all_to_all(send, ("seq", "batch"), 0, 0, tiled=True)
    recv = recv.reshape(seq_count, batch_count, width).transpose(1, 2, 0)
    sig_rows = recv[:, :group].reshape(batch_count * group, seq_count)
    cot_rows = recv[:, group : 2 * group].reshape(batch_count * group, seq_count)
    filt_rows = recv[:, 2 * group :].reshape(group, seq_count)
    half = group // 2
    z_real = jnp.concatenate([sig_rows, filt_rows[:half]], axis=0)
    z_imag = jnp.concatenate([cot_rows, filt_rows[half:]], axis=0)
    rows = z_real.shape[0]

    k1_count = 2 * seq_count
    both = contract("ap,pm->am", jnp.concatenate([z_real, z_imag], axis=0), forward_p)
    a_real = both[:rows, :k1_count] + both[rows:, k1_count:]
    a_imag = both[rows:, :k1_count] - both[:rows, k1_count:]
    k1_all = jnp.asarray(pairs.reshape(-1))
    angle = ((me * k1_all) % total_len).astype(f32) * (2.0 * np.pi / total_len)
    a_real, a_imag = turn(a_real, a_imag, angle[None, :], -1.0)
    stacked = jnp.stack([a_real, a_imag]).reshape(2, rows, seq_count, 2)
    cols = lax.all_to_all(stacked, "seq", 2, 2, tiled=True)

    cols = cols.transpose(0, 1, 3, 2).reshape(2 * rows * 2, seq_count)
    spec = contract("aj,jm->am", cols, local).reshape(2, rows, 2, 2 * seq_count)
    z_re = spec[0, :, :, :seq_count] + spec[1, :, :, seq_count:]
    z_im = spec[1, :, :, :seq_count] - spec[0, :, :, seq_count:]

    flip_re = z_re[:, ::-1, ::-1]
    flip_im = z_im[:, ::-1, ::-1]
    zero_re = jnp.stack([jnp.roll(z_re[:, 0, ::-1], 1, axis=-1), z_re[:, 1, ::-1]], axis=1)
    zero_im = jnp.stack([jnp.roll(z_im[:, 0, ::-1], 1, axis=-1), z_im[:, 1, ::-1]], axis=1)
    at_zero = me == 0
    p_re = jnp.where(at_zero, zero_re, flip_re)
    p_im = -jnp.where(at_zero, zero_im, flip_im)
    first_re = 0.5 * (z_re + p_re)
    first_im = 0.5 * (z_im + p_im)
    second_re = 0.5 * (z_im - p_im)
    second_im = -0.5 * (z_re - p_re)

    sig_count = batch_count * group
    x_re = first_re[:sig_count].reshape(batch_count, group, 2, seq_count)
    x_im = first_im[:sig_count].reshape(batch_count, group, 2, seq_count)
    d_re = second_re[:sig_count].reshape(batch_count, group, 2, seq_count)
    d_im = second_im[:sig_count].reshape(batch_count, group, 2, seq_count)
    h_re = jnp.concatenate([first_re[sig_count:], second_re[sig_count:]], axis=0)
    h_im = jnp.concatenate([first_im[sig_count:], second_im[sig_count:]], axis=0)

    gx_re = h_re * d_re + h_im * d_im
    gx_im = h_re * d_im - h_im * d_re
    gh_re = jnp.sum(x_re * d_re + x_im * d_im, axis=0)
    gh_im = jnp.sum(x_re * d_im - x_im * d_re, axis=0)
    gx_re = gx_re.reshape(sig_count, 2, seq_count)
    gx_im = gx_im.reshape(sig_count, 2, seq_count)
    sig_half = sig_count // 2
    q_re = jnp.concatenate([gx_re[:sig_half] - gx_im[sig_half:], gh_re[:half] - gh_im[half:]], axis=0)
    q_im = jnp.concatenate([gx_im[:sig_half] + gx_re[sig_half:], gh_im[:half] + gh_re[half:]], axis=0)
    back_rows = q_re.shape[0]

    both = contract(
        "ak,km->am", jnp.concatenate([q_re, q_im], axis=0).reshape(2 * back_rows * 2, seq_count), local
    ).reshape(2, back_rows, 2, 2 * seq_count)
    b_re = both[0, :, :, :seq_count] - both[1, :, :, seq_count:]
    b_im = both[1, :, :, :seq_count] + both[0, :, :, seq_count:]
    held = lax.dynamic_index_in_dim(jnp.asarray(pairs), me, axis=0, keepdims=False)
    j_index = jnp.arange(seq_count, dtype=jnp.int32)
    angle = ((held[:, None] * j_index[None, :]) % total_len).astype(f32) * (2.0 * np.pi / total_len)
    b_re, b_im = turn(b_re, b_im, angle[None], 1.0)
    gathered = lax.all_to_all(jnp.stack([b_re, b_im]), "seq", 3, 3, tiled=True)

    out = contract("ak,km->am", gathered.reshape(2 * back_rows, 2 * seq_count), inverse_p)
    out_re = out[:back_rows, :seq_count] - out[back_rows:, seq_count:]
    out_im = out[back_rows:, :seq_count] + out[:back_rows, seq_count:]
    in_rows = jnp.concatenate([out_re[:sig_half], out_im[:sig_half]], axis=0)
    filt_out = jnp.concatenate([out_re[sig_half:], out_im[sig_half:]], axis=0)

    ig = in_rows.reshape(batch_count, group, seq_count).transpose(2, 0, 1)
    fg = jnp.broadcast_to(filt_out.T[:, None, :], (seq_count, batch_count, group))
    send = jnp.concatenate([ig, fg], axis=2).reshape(seq_count * batch_count, 2 * group)
    recv = lax.all_to_all(send, ("seq", "batch"), 0, 0, tiled=True)
    recv = recv.reshape(seq_count, batch_count, 2 * group).transpose(1, 2, 0)
    in_grad = recv[:, :group].reshape(channels, seq_count)
    filter_grad = recv[:, group:].reshape(channels, seq_count)
    return (in_grad.astype(jnp.bfloat16)[None], filter_grad)


def solution(mesh):
    placed = (P("batch", None, "seq"), P("batch", None, "seq"), P(None, "seq"))
    return jax.shard_map(
        body,
        mesh=mesh,
        in_specs=placed,
        out_specs=(P("batch", None, "seq"), P(None, "seq")),
        check_vma=False,
    )
```

```python
import numpy as np

import jax
import jax.numpy as jnp
from jax import lax
from jax.sharding import PartitionSpec as P


def contract(left, right):
    return jnp.matmul(
        left, right, precision=lax.Precision.HIGHEST, preferred_element_type=jnp.float32
    )


def tables(outer, inner, used):
    total = outer * inner
    k1 = np.arange(outer)
    theta1 = 2.0 * np.pi * np.outer(k1, np.arange(used)) / outer
    first = np.concatenate([np.cos(theta1), np.sin(theta1)], axis=0)
    back = np.concatenate([np.cos(theta1).T, np.sin(theta1).T], axis=0) / total
    phi = 2.0 * np.pi * np.outer(k1, np.arange(inner)) / total
    k2 = np.arange(inner)
    theta2 = 2.0 * np.pi * np.outer(k2, k2) / inner
    second = np.concatenate([np.cos(theta2), np.sin(theta2)], axis=1)
    as32 = lambda a: jnp.asarray(a.astype(np.float32))
    return as32(first), as32(back), as32(np.cos(phi)), as32(np.sin(phi)), as32(second)


def partner(values):
    flipped = jnp.roll(values[::-1, ::-1], 1, axis=0)
    row0 = jnp.roll(values[0, ::-1], 1)
    return flipped.at[0].set(row0)


def body(inputs, out_grad, filters):
    seq_count = lax.axis_size("seq")
    batch_count = lax.axis_size("batch")
    mine = lax.axis_index("batch")
    channels = inputs.shape[1]
    length_dev = inputs.shape[2]
    assert channels == seq_count and inputs.shape[0] == 1
    length = seq_count * length_dev
    total = 2 * length
    inner = 2 * length_dev
    outer = total // inner
    used = length // inner
    first, back, tw_cos, tw_sin, second = tables(outer, inner, used)
    f32 = jnp.float32

    send = jnp.stack([inputs[0].astype(f32), out_grad[0].astype(f32), filters], axis=1)
    recv = lax.all_to_all(send, "seq", 0, 0, tiled=True)
    signal = recv[:, 0].reshape(used, inner)
    cotangent = recv[:, 1].reshape(used, inner)
    filt = recv[:, 2].reshape(used, inner)

    stage = contract(first, jnp.concatenate([signal, cotangent, filt], axis=1))
    cos_part, sin_part = stage[:outer], stage[outer:]
    z_re = cos_part[:, :inner] + sin_part[:, inner : 2 * inner]
    z_im = cos_part[:, inner : 2 * inner] - sin_part[:, :inner]
    h_re = cos_part[:, 2 * inner :]
    h_im = -sin_part[:, 2 * inner :]

    def twist(re, im, orient):
        return re * tw_cos - orient * im * tw_sin, im * tw_cos + orient * re * tw_sin

    z_re, z_im = twist(z_re, z_im, -1.0)
    h_re, h_im = twist(h_re, h_im, -1.0)

    stage = contract(jnp.concatenate([z_re, z_im, h_re, h_im], axis=0), second)
    c2, s2 = stage[:, :inner], stage[:, inner:]
    zr = c2[:outer] + s2[outer : 2 * outer]
    zi = c2[outer : 2 * outer] - s2[:outer]
    hr = c2[2 * outer : 3 * outer] + s2[3 * outer :]
    hi = c2[3 * outer :] - s2[2 * outer : 3 * outer]

    pr = partner(zr)
    pi = -partner(zi)
    xr = 0.5 * (zr + pr)
    xi = 0.5 * (zi + pi)
    dr = 0.5 * (zi - pi)
    di = -0.5 * (zr - pr)

    gx_re = hr * dr + hi * di
    gx_im = hr * di - hi * dr
    gh_re = xr * dr + xi * di
    gh_im = xr * di - xi * dr
    q_re = gx_re - gh_im
    q_im = gx_im + gh_re

    stage = contract(jnp.concatenate([q_re, q_im], axis=0), second)
    c2, s2 = stage[:, :inner], stage[:, inner:]
    g_re = c2[:outer] - s2[outer:]
    g_im = c2[outer:] + s2[:outer]
    g_re, g_im = twist(g_re, g_im, 1.0)
    stage = contract(back, jnp.concatenate([g_re, g_im], axis=1))
    c1, s1 = stage[:used], stage[used:]
    in_row = c1[:, :inner] - s1[:, inner:]
    filt_row = c1[:, inner:] + s1[:, :inner]

    in_blocks = in_row.reshape(seq_count, length_dev)
    filt_blocks = filt_row.reshape(seq_count, length_dev)
    own = (jnp.arange(batch_count) == mine)[None, :, None]
    send = jnp.concatenate(
        [
            jnp.where(own, in_blocks[:, None, :], 0.0),
            jnp.broadcast_to(filt_blocks[:, None, :], (seq_count, batch_count, length_dev)),
        ],
        axis=2,
    ).reshape(seq_count * batch_count, 2 * length_dev)
    recv = lax.all_to_all(send, ("seq", "batch"), 0, 0, tiled=True)
    recv = recv.reshape(seq_count, batch_count, 2 * length_dev)
    in_grad = lax.dynamic_index_in_dim(recv[:, :, :length_dev], mine, axis=1, keepdims=False)
    parts = recv[:, :, length_dev:]
    filter_grad = parts[:, 0]
    for index in range(1, batch_count):
        filter_grad = filter_grad + parts[:, index]
    return (in_grad.astype(jnp.bfloat16)[None], filter_grad)


def solution(mesh):
    placed = (P("batch", None, "seq"), P("batch", None, "seq"), P(None, "seq"))
    return jax.shard_map(
        body,
        mesh=mesh,
        in_specs=placed,
        out_specs=(P("batch", None, "seq"), P(None, "seq")),
        check_vma=False,
    )
```

```python
import numpy as np

import jax
import jax.numpy as jnp
from jax import lax
from jax.sharding import PartitionSpec as P


def contract(left, right):
    return jnp.matmul(
        left, right, precision=lax.Precision.HIGHEST, preferred_element_type=jnp.float32
    )


def tables(outer, inner, used):
    total = outer * inner
    k1 = np.arange(outer)
    theta1 = 2.0 * np.pi * np.outer(k1, np.arange(used)) / outer
    first = np.concatenate([np.cos(theta1), np.sin(theta1)], axis=0)
    back = np.concatenate([np.cos(theta1).T, np.sin(theta1).T], axis=0) / total
    phi = 2.0 * np.pi * np.outer(k1, np.arange(inner)) / total
    k2 = np.arange(inner)
    theta2 = 2.0 * np.pi * np.outer(k2, k2) / inner
    second = np.concatenate([np.cos(theta2), np.sin(theta2)], axis=1)
    as32 = lambda a: jnp.asarray(a.astype(np.float32))
    return as32(first), as32(back), as32(np.cos(phi)), as32(np.sin(phi)), as32(second)


def partner(values):
    flipped = jnp.roll(values[::-1, ::-1], 1, axis=0)
    row0 = jnp.roll(values[0, ::-1], 1)
    return flipped.at[0].set(row0)


def body(inputs, out_grad, filters):
    seq_count = lax.axis_size("seq")
    batch_count = lax.axis_size("batch")
    mine = lax.axis_index("batch")
    channels = inputs.shape[1]
    length_dev = inputs.shape[2]
    assert channels == seq_count and inputs.shape[0] == 1
    length = seq_count * length_dev
    total = 2 * length
    inner = 2 * length_dev
    outer = total // inner
    used = length // inner
    first, back, tw_cos, tw_sin, second = tables(outer, inner, used)
    f32 = jnp.float32

    send = jnp.stack([inputs[0].astype(f32), out_grad[0].astype(f32), filters], axis=1)
    recv = lax.all_to_all(send, "seq", 0, 0, tiled=True)
    signal = recv[:, 0].reshape(used, inner)
    cotangent = recv[:, 1].reshape(used, inner)
    filt = recv[:, 2].reshape(used, inner)

    stage = contract(first, jnp.concatenate([signal, cotangent, filt], axis=1))
    cos_part, sin_part = stage[:outer], stage[outer:]
    z_re = cos_part[:, :inner] + sin_part[:, inner : 2 * inner]
    z_im = cos_part[:, inner : 2 * inner] - sin_part[:, :inner]
    h_re = cos_part[:, 2 * inner :]
    h_im = -sin_part[:, 2 * inner :]

    def twist(re, im, orient):
        return re * tw_cos - orient * im * tw_sin, im * tw_cos + orient * re * tw_sin

    z_re, z_im = twist(z_re, z_im, -1.0)
    h_re, h_im = twist(h_re, h_im, -1.0)

    stage = contract(jnp.concatenate([z_re, z_im, h_re, h_im], axis=0), second)
    c2, s2 = stage[:, :inner], stage[:, inner:]
    zr = c2[:outer] + s2[outer : 2 * outer]
    zi = c2[outer : 2 * outer] - s2[:outer]
    hr = c2[2 * outer : 3 * outer] + s2[3 * outer :]
    hi = c2[3 * outer :] - s2[2 * outer : 3 * outer]

    pr = partner(zr)
    pi = -partner(zi)
    xr = 0.5 * (zr + pr)
    xi = 0.5 * (zi + pi)
    dr = 0.5 * (zi - pi)
    di = -0.5 * (zr - pr)

    gx_re = hr * dr + hi * di
    gx_im = hr * di - hi * dr
    gh_re = xr * dr + xi * di
    gh_im = xr * di - xi * dr
    q_re = gx_re - gh_im
    q_im = gx_im + gh_re

    stage = contract(jnp.concatenate([q_re, q_im], axis=0), second)
    c2, s2 = stage[:, :inner], stage[:, inner:]
    g_re = c2[:outer] - s2[outer:]
    g_im = c2[outer:] + s2[:outer]
    g_re, g_im = twist(g_re, g_im, 1.0)
    stage = contract(back, jnp.concatenate([g_re, g_im], axis=1))
    c1, s1 = stage[:used], stage[used:]
    in_row = c1[:, :inner] - s1[:, inner:]
    filt_row = c1[:, inner:] + s1[:, :inner]

    assert batch_count & (batch_count - 1) == 0
    step = 1
    while step < batch_count:
        pairs = [(index, index ^ step) for index in range(batch_count)]
        filt_row = filt_row + lax.ppermute(filt_row, "batch", pairs)
        step *= 2

    send = jnp.concatenate(
        [in_row.reshape(seq_count, length_dev), filt_row.reshape(seq_count, length_dev)], axis=1
    )
    recv = lax.all_to_all(send, "seq", 0, 0, tiled=True)
    in_grad = recv[:, :length_dev]
    filter_grad = recv[:, length_dev:]
    return (in_grad.astype(jnp.bfloat16)[None], filter_grad)


def solution(mesh):
    placed = (P("batch", None, "seq"), P("batch", None, "seq"), P(None, "seq"))
    return jax.shard_map(
        body,
        mesh=mesh,
        in_specs=placed,
        out_specs=(P("batch", None, "seq"), P(None, "seq")),
        check_vma=False,
    )
```

```python
import numpy as np

import jax
import jax.numpy as jnp
from jax import lax
from jax.sharding import PartitionSpec as P


def contract(left, right):
    return jnp.matmul(
        left, right, precision=lax.Precision.HIGHEST, preferred_element_type=jnp.float32
    )


def tables(outer, inner, used):
    total = outer * inner
    k1 = np.arange(outer)
    theta1 = 2.0 * np.pi * np.outer(k1, np.arange(used)) / outer
    first = np.concatenate([np.cos(theta1), np.sin(theta1)], axis=0)
    back = np.concatenate([np.cos(theta1).T, np.sin(theta1).T], axis=0) / total
    phi = 2.0 * np.pi * np.outer(k1, np.arange(inner)) / total
    k2 = np.arange(inner)
    theta2 = 2.0 * np.pi * np.outer(k2, k2) / inner
    second = np.concatenate([np.cos(theta2), np.sin(theta2)], axis=1)
    as32 = lambda a: jnp.asarray(a.astype(np.float32))
    return as32(first), as32(back), as32(np.cos(phi)), as32(np.sin(phi)), as32(second)


def body(inputs, out_grad, filters):
    seq_count = lax.axis_size("seq")
    batch_count = lax.axis_size("batch")
    mine = lax.axis_index("batch")
    channels = inputs.shape[1]
    length_dev = inputs.shape[2]
    assert channels == seq_count and inputs.shape[0] == 1
    length = seq_count * length_dev
    total = 2 * length
    inner = 2 * length_dev
    outer = total // inner
    used = length // inner
    first, back, tw_cos, tw_sin, second = tables(outer, inner, used)
    f32 = jnp.float32

    send = jnp.stack([inputs[0].astype(f32), out_grad[0].astype(f32), filters], axis=1)
    recv = lax.all_to_all(send, "seq", 0, 0, tiled=True)
    signal = recv[:, 0].reshape(used, inner)
    cotangent = recv[:, 1].reshape(used, inner)
    filt = recv[:, 2].reshape(used, inner)

    stage = contract(first, jnp.concatenate([signal, cotangent, filt], axis=1))
    cos_part, sin_part = stage[:outer], stage[outer:]

    def twist(re, im, orient):
        return re * tw_cos - orient * im * tw_sin, im * tw_cos + orient * re * tw_sin

    parts = []
    for index in range(3):
        cut = slice(index * inner, (index + 1) * inner)
        parts.extend(twist(cos_part[:, cut], -sin_part[:, cut], -1.0))

    stage = contract(jnp.concatenate(parts, axis=0), second)
    c2, s2 = stage[:, :inner], stage[:, inner:]
    spectra = []
    for index in range(3):
        re_rows = slice(2 * index * outer, (2 * index + 1) * outer)
        im_rows = slice((2 * index + 1) * outer, (2 * index + 2) * outer)
        spectra.append((c2[re_rows] + s2[im_rows], c2[im_rows] - s2[re_rows]))
    (xr, xi), (dr, di), (hr, hi) = spectra

    gx_re = hr * dr + hi * di
    gx_im = hr * di - hi * dr
    gh_re = xr * dr + xi * di
    gh_im = xr * di - xi * dr
    q_re = gx_re - gh_im
    q_im = gx_im + gh_re

    stage = contract(jnp.concatenate([q_re, q_im], axis=0), second)
    c2, s2 = stage[:, :inner], stage[:, inner:]
    g_re = c2[:outer] - s2[outer:]
    g_im = c2[outer:] + s2[:outer]
    g_re, g_im = twist(g_re, g_im, 1.0)
    stage = contract(back, jnp.concatenate([g_re, g_im], axis=1))
    c1, s1 = stage[:used], stage[used:]
    in_row = c1[:, :inner] - s1[:, inner:]
    filt_row = c1[:, inner:] + s1[:, :inner]

    assert batch_count & (batch_count - 1) == 0
    step = 1
    while step < batch_count:
        pairs = [(index, index ^ step) for index in range(batch_count)]
        filt_row = filt_row + lax.ppermute(filt_row, "batch", pairs)
        step *= 2

    send = jnp.concatenate(
        [in_row.reshape(seq_count, length_dev), filt_row.reshape(seq_count, length_dev)], axis=1
    )
    recv = lax.all_to_all(send, "seq", 0, 0, tiled=True)
    in_grad = recv[:, :length_dev]
    filter_grad = recv[:, length_dev:]
    return (in_grad.astype(jnp.bfloat16)[None], filter_grad)


def solution(mesh):
    placed = (P("batch", None, "seq"), P("batch", None, "seq"), P(None, "seq"))
    return jax.shard_map(
        body,
        mesh=mesh,
        in_specs=placed,
        out_specs=(P("batch", None, "seq"), P(None, "seq")),
        check_vma=False,
    )
```

```python
import numpy as np

import jax
import jax.numpy as jnp
from jax import lax
from jax.sharding import PartitionSpec as P


def contract(left, right):
    return jnp.matmul(
        left, right, precision=lax.Precision.HIGHEST, preferred_element_type=jnp.float32
    )


def tables(outer, inner, used):
    total = outer * inner
    k1 = np.arange(outer)
    theta1 = 2.0 * np.pi * np.outer(k1, np.arange(used)) / outer
    first = np.concatenate([np.cos(theta1), np.sin(theta1)], axis=0)
    back = np.concatenate([np.cos(theta1).T, np.sin(theta1).T], axis=0) / total
    phi = 2.0 * np.pi * np.outer(k1, np.arange(inner)) / total
    k2 = np.arange(inner)
    theta2 = 2.0 * np.pi * np.outer(k2, k2) / inner
    second = np.concatenate([np.cos(theta2), np.sin(theta2)], axis=1)
    as32 = lambda a: jnp.asarray(a.astype(np.float32))
    return as32(first), as32(back), as32(np.cos(phi)), as32(np.sin(phi)), as32(second)


def body(inputs, out_grad, filters):
    seq_count = lax.axis_size("seq")
    batch_count = lax.axis_size("batch")
    mine = lax.axis_index("batch")
    channels = inputs.shape[1]
    length_dev = inputs.shape[2]
    assert channels == seq_count and inputs.shape[0] == 1
    length = seq_count * length_dev
    total = 2 * length
    inner = 2 * length_dev
    outer = total // inner
    used = length // inner
    first, back, tw_cos, tw_sin, second = tables(outer, inner, used)
    f32 = jnp.float32

    send = jnp.stack([inputs[0].astype(f32), out_grad[0].astype(f32), filters], axis=1)
    send = send.reshape(channels, 1, 3 * length_dev)
    recv = lax.all_to_all(send, "seq", 0, 0, tiled=True)
    recv = recv.reshape(seq_count, 3, length_dev)
    signal = recv[:, 0].reshape(used, inner)
    cotangent = recv[:, 1].reshape(used, inner)
    filt = recv[:, 2].reshape(used, inner)

    stage = contract(first, jnp.concatenate([signal, cotangent, filt], axis=1))
    cos_part, sin_part = stage[:outer], stage[outer:]

    def twist(re, im, orient):
        return re * tw_cos - orient * im * tw_sin, im * tw_cos + orient * re * tw_sin

    parts = []
    for index in range(3):
        cut = slice(index * inner, (index + 1) * inner)
        parts.extend(twist(cos_part[:, cut], -sin_part[:, cut], -1.0))

    stage = contract(jnp.concatenate(parts, axis=0), second)
    c2, s2 = stage[:, :inner], stage[:, inner:]
    spectra = []
    for index in range(3):
        re_rows = slice(2 * index * outer, (2 * index + 1) * outer)
        im_rows = slice((2 * index + 1) * outer, (2 * index + 2) * outer)
        spectra.append((c2[re_rows] + s2[im_rows], c2[im_rows] - s2[re_rows]))
    (xr, xi), (dr, di), (hr, hi) = spectra

    gx_re = hr * dr + hi * di
    gx_im = hr * di - hi * dr
    gh_re = xr * dr + xi * di
    gh_im = xr * di - xi * dr
    q_re = gx_re - gh_im
    q_im = gx_im + gh_re

    stage = contract(jnp.concatenate([q_re, q_im], axis=0), second)
    c2, s2 = stage[:, :inner], stage[:, inner:]
    g_re = c2[:outer] - s2[outer:]
    g_im = c2[outer:] + s2[:outer]
    g_re, g_im = twist(g_re, g_im, 1.0)
    stage = contract(back, jnp.concatenate([g_re, g_im], axis=1))
    c1, s1 = stage[:used], stage[used:]
    in_row = c1[:, :inner] - s1[:, inner:]
    filt_row = c1[:, inner:] + s1[:, :inner]

    received = [filt_row]
    for step in range(1, batch_count):
        pairs = [(index, index ^ step) for index in range(batch_count)]
        received.append(lax.ppermute(filt_row, "batch", pairs))
    ordered = []
    for source in range(batch_count):
        pick = received[0]
        for step in range(1, batch_count):
            pick = jnp.where((mine ^ step) == source, received[step], pick)
        ordered.append(pick)
    filt_row = ordered[0]
    for source in range(1, batch_count):
        filt_row = filt_row + ordered[source]

    send = jnp.concatenate(
        [in_row.reshape(seq_count, length_dev), filt_row.reshape(seq_count, length_dev)], axis=1
    )
    recv = lax.all_to_all(send, "seq", 0, 0, tiled=True)
    in_grad = recv[:, :length_dev]
    filter_grad = recv[:, length_dev:]
    return (in_grad.astype(jnp.bfloat16)[None], filter_grad)


def solution(mesh):
    placed = (P("batch", None, "seq"), P("batch", None, "seq"), P(None, "seq"))
    return jax.shard_map(
        body,
        mesh=mesh,
        in_specs=placed,
        out_specs=(P("batch", None, "seq"), P(None, "seq")),
        check_vma=False,
    )
```

```python
import numpy as np

import jax
import jax.numpy as jnp
from jax import lax
from jax.sharding import PartitionSpec as P


def contract(left, right):
    return jnp.matmul(
        left, right, precision=lax.Precision.HIGH, preferred_element_type=jnp.float32
    )


def tables(outer, inner, used):
    total = outer * inner
    k1 = np.arange(outer)
    theta1 = 2.0 * np.pi * np.outer(k1, np.arange(used)) / outer
    first = np.concatenate([np.cos(theta1), np.sin(theta1)], axis=0)
    back = np.concatenate([np.cos(theta1).T, np.sin(theta1).T], axis=0) / total
    phi = 2.0 * np.pi * np.outer(k1, np.arange(inner)) / total
    k2 = np.arange(inner)
    theta2 = 2.0 * np.pi * np.outer(k2, k2) / inner
    second = np.concatenate([np.cos(theta2), np.sin(theta2)], axis=1)
    as32 = lambda a: jnp.asarray(a.astype(np.float32))
    return as32(first), as32(back), as32(np.cos(phi)), as32(np.sin(phi)), as32(second)


def body(inputs, out_grad, filters):
    seq_count = lax.axis_size("seq")
    batch_count = lax.axis_size("batch")
    mine = lax.axis_index("batch")
    channels = inputs.shape[1]
    length_dev = inputs.shape[2]
    assert channels == seq_count and inputs.shape[0] == 1
    length = seq_count * length_dev
    total = 2 * length
    inner = 2 * length_dev
    outer = total // inner
    used = length // inner
    first, back, tw_cos, tw_sin, second = tables(outer, inner, used)
    f32 = jnp.float32

    send = jnp.concatenate([inputs[0], out_grad[0]], axis=1).astype(f32)
    send = jnp.concatenate([send, filters], axis=1).reshape(channels, 1, 3 * length_dev)
    recv = lax.all_to_all(send, "seq", 0, 0, tiled=True)
    recv = recv.reshape(seq_count, 3, length_dev)
    signal = recv[:, 0].reshape(used, inner)
    cotangent = recv[:, 1].reshape(used, inner)
    filt = recv[:, 2].reshape(used, inner)

    stage = contract(first, jnp.concatenate([signal, cotangent, filt], axis=1))
    cos_part, sin_part = stage[:outer], stage[outer:]

    def twist(re, im, orient):
        return re * tw_cos - orient * im * tw_sin, im * tw_cos + orient * re * tw_sin

    parts = []
    for index in range(3):
        cut = slice(index * inner, (index + 1) * inner)
        parts.extend(twist(cos_part[:, cut], -sin_part[:, cut], -1.0))

    stage = contract(jnp.concatenate(parts, axis=0), second)
    c2, s2 = stage[:, :inner], stage[:, inner:]
    spectra = []
    for index in range(3):
        re_rows = slice(2 * index * outer, (2 * index + 1) * outer)
        im_rows = slice((2 * index + 1) * outer, (2 * index + 2) * outer)
        spectra.append((c2[re_rows] + s2[im_rows], c2[im_rows] - s2[re_rows]))
    (xr, xi), (dr, di), (hr, hi) = spectra

    gx_re = hr * dr + hi * di
    gx_im = hr * di - hi * dr
    gh_re = xr * dr + xi * di
    gh_im = xr * di - xi * dr
    q_re = gx_re - gh_im
    q_im = gx_im + gh_re

    stage = contract(jnp.concatenate([q_re, q_im], axis=0), second)
    c2, s2 = stage[:, :inner], stage[:, inner:]
    g_re = c2[:outer] - s2[outer:]
    g_im = c2[outer:] + s2[:outer]
    g_re, g_im = twist(g_re, g_im, 1.0)
    stage = contract(back, jnp.concatenate([g_re, g_im], axis=1))
    c1, s1 = stage[:used], stage[used:]
    in_row = c1[:, :inner] - s1[:, inner:]
    filt_row = c1[:, inner:] + s1[:, :inner]

    received = [filt_row]
    for step in range(1, batch_count):
        pairs = [(index, index ^ step) for index in range(batch_count)]
        received.append(lax.ppermute(filt_row, "batch", pairs))
    ordered = []
    for source in range(batch_count):
        pick = received[0]
        for step in range(1, batch_count):
            pick = jnp.where((mine ^ step) == source, received[step], pick)
        ordered.append(pick)
    filt_row = ordered[0]
    for source in range(1, batch_count):
        filt_row = filt_row + ordered[source]

    send = jnp.concatenate(
        [in_row.reshape(seq_count, length_dev), filt_row.reshape(seq_count, length_dev)], axis=1
    )
    recv = lax.all_to_all(send, "seq", 0, 0, tiled=True)
    in_grad = recv[:, :length_dev]
    filter_grad = recv[:, length_dev:]
    return (in_grad.astype(jnp.bfloat16)[None], filter_grad)


def solution(mesh):
    placed = (P("batch", None, "seq"), P("batch", None, "seq"), P(None, "seq"))
    return jax.shard_map(
        body,
        mesh=mesh,
        in_specs=placed,
        out_specs=(P("batch", None, "seq"), P(None, "seq")),
        check_vma=False,
    )
```

```python
import numpy as np

import jax
import jax.numpy as jnp
from jax import lax
from jax.sharding import PartitionSpec as P


def contract(left, right):
    return jnp.matmul(
        left, right, precision=lax.Precision.HIGH, preferred_element_type=jnp.float32
    )


def tables(outer, inner, used):
    total = outer * inner
    k1 = np.arange(outer)
    theta1 = 2.0 * np.pi * np.outer(k1, np.arange(used)) / outer
    first = np.concatenate([np.cos(theta1), np.sin(theta1)], axis=0)
    back = np.concatenate([np.cos(theta1).T, np.sin(theta1).T], axis=0) / total
    phi = 2.0 * np.pi * np.outer(k1, np.arange(inner)) / total
    k2 = np.arange(inner)
    theta2 = 2.0 * np.pi * np.outer(k2, k2) / inner
    second = np.concatenate([np.cos(theta2), np.sin(theta2)], axis=1)
    as32 = lambda a: jnp.asarray(a.astype(np.float32))
    return as32(first), as32(back), as32(np.cos(phi)), as32(np.sin(phi)), as32(second)


def body(inputs, out_grad, filters):
    seq_count = lax.axis_size("seq")
    batch_count = lax.axis_size("batch")
    mine = lax.axis_index("batch")
    channels = inputs.shape[1]
    length_dev = inputs.shape[2]
    assert channels == seq_count and inputs.shape[0] == 1
    length = seq_count * length_dev
    total = 2 * length
    inner = 2 * length_dev
    outer = total // inner
    used = length // inner
    first, back, tw_cos, tw_sin, second = tables(outer, inner, used)
    f32 = jnp.float32

    send = jnp.concatenate([inputs[0], out_grad[0]], axis=1).astype(f32)
    send = jnp.concatenate([send, filters], axis=1).reshape(channels, 1, 3 * length_dev)
    recv = lax.all_to_all(send, "seq", 0, 0, tiled=True)
    recv = recv.reshape(seq_count, 3, length_dev)
    signal = recv[:, 0].reshape(used, inner)
    cotangent = recv[:, 1].reshape(used, inner)
    filt = recv[:, 2].reshape(used, inner)

    stage = contract(first, jnp.concatenate([signal, cotangent, filt], axis=1))
    cos_part, sin_part = stage[:outer], stage[outer:]

    def twist(re, im, orient):
        return re * tw_cos - orient * im * tw_sin, im * tw_cos + orient * re * tw_sin

    parts = []
    for index in range(3):
        cut = slice(index * inner, (index + 1) * inner)
        parts.extend(twist(cos_part[:, cut], -sin_part[:, cut], -1.0))

    stage = contract(jnp.concatenate(parts, axis=0), second)
    c2, s2 = stage[:, :inner], stage[:, inner:]
    spectra = []
    for index in range(3):
        re_rows = slice(2 * index * outer, (2 * index + 1) * outer)
        im_rows = slice((2 * index + 1) * outer, (2 * index + 2) * outer)
        spectra.append((c2[re_rows] + s2[im_rows], c2[im_rows] - s2[re_rows]))
    (xr, xi), (dr, di), (hr, hi) = spectra

    gx_re = hr * dr + hi * di
    gx_im = hr * di - hi * dr
    gh_re = xr * dr + xi * di
    gh_im = xr * di - xi * dr
    q_re = gx_re - gh_im
    q_im = gx_im + gh_re

    stage = contract(jnp.concatenate([q_re, q_im], axis=0), second)
    c2, s2 = stage[:, :inner], stage[:, inner:]
    g_re = c2[:outer] - s2[outer:]
    g_im = c2[outer:] + s2[:outer]
    g_re, g_im = twist(g_re, g_im, 1.0)
    stage = contract(back, jnp.concatenate([g_re, g_im], axis=1))
    c1, s1 = stage[:used], stage[used:]
    in_row = c1[:, :inner] - s1[:, inner:]
    filt_row = c1[:, inner:] + s1[:, :inner]

    spread = jnp.broadcast_to(filt_row[None], (batch_count,) + filt_row.shape)
    gathered = lax.all_to_all(spread, "batch", 0, 0, tiled=True)
    filt_row = gathered[0]
    for source in range(1, batch_count):
        filt_row = filt_row + gathered[source]

    send = jnp.concatenate(
        [in_row.reshape(seq_count, length_dev), filt_row.reshape(seq_count, length_dev)], axis=1
    )
    recv = lax.all_to_all(send, "seq", 0, 0, tiled=True)
    in_grad = recv[:, :length_dev]
    filter_grad = recv[:, length_dev:]
    return (in_grad.astype(jnp.bfloat16)[None], filter_grad)


def solution(mesh):
    placed = (P("batch", None, "seq"), P("batch", None, "seq"), P(None, "seq"))
    return jax.shard_map(
        body,
        mesh=mesh,
        in_specs=placed,
        out_specs=(P("batch", None, "seq"), P(None, "seq")),
        check_vma=False,
    )
```

```python
import numpy as np

import jax
import jax.numpy as jnp
from jax import lax
from jax.sharding import Mesh, PartitionSpec as P


def contract(left, right):
    return jnp.matmul(
        left, right, precision=lax.Precision.HIGH, preferred_element_type=jnp.float32
    )


def tables(outer, inner, used):
    total = outer * inner
    k1 = np.arange(outer)
    theta1 = 2.0 * np.pi * np.outer(k1, np.arange(used)) / outer
    first = np.concatenate([np.cos(theta1), np.sin(theta1)], axis=0)
    back = np.concatenate([np.cos(theta1).T, np.sin(theta1).T], axis=0) / total
    phi = 2.0 * np.pi * np.outer(k1, np.arange(inner)) / total
    k2 = np.arange(inner)
    theta2 = 2.0 * np.pi * np.outer(k2, k2) / inner
    second = np.concatenate([np.cos(theta2), np.sin(theta2)], axis=1)
    as32 = lambda a: jnp.asarray(a.astype(np.float32))
    return as32(first), as32(back), as32(np.cos(phi)), as32(np.sin(phi)), as32(second)


def body(inputs, out_grad, filters):
    seq_count = lax.axis_size("seq")
    channels = inputs.shape[1]
    length_dev = inputs.shape[2]
    assert channels == seq_count and inputs.shape[0] == 1
    length = seq_count * length_dev
    total = 2 * length
    inner = 2 * length_dev
    outer = total // inner
    used = length // inner
    first, back, tw_cos, tw_sin, second = tables(outer, inner, used)
    f32 = jnp.float32

    send = jnp.concatenate([inputs[0], out_grad[0]], axis=1).astype(f32)
    send = jnp.concatenate([send, filters], axis=1).reshape(channels, 1, 3 * length_dev)
    recv = lax.all_to_all(send, "seq", 0, 0, tiled=True)
    recv = recv.reshape(seq_count, 3, length_dev)
    signal = recv[:, 0].reshape(used, inner)
    cotangent = recv[:, 1].reshape(used, inner)
    filt = recv[:, 2].reshape(used, inner)

    stage = contract(first, jnp.concatenate([signal, cotangent, filt], axis=1))
    cos_part, sin_part = stage[:outer], stage[outer:]

    def twist(re, im, orient):
        return re * tw_cos - orient * im * tw_sin, im * tw_cos + orient * re * tw_sin

    parts = []
    for index in range(3):
        cut = slice(index * inner, (index + 1) * inner)
        parts.extend(twist(cos_part[:, cut], -sin_part[:, cut], -1.0))

    stage = contract(jnp.concatenate(parts, axis=0), second)
    c2, s2 = stage[:, :inner], stage[:, inner:]
    spectra = []
    for index in range(3):
        re_rows = slice(2 * index * outer, (2 * index + 1) * outer)
        im_rows = slice((2 * index + 1) * outer, (2 * index + 2) * outer)
        spectra.append((c2[re_rows] + s2[im_rows], c2[im_rows] - s2[re_rows]))
    (xr, xi), (dr, di), (hr, hi) = spectra

    gx_re = hr * dr + hi * di
    gx_im = hr * di - hi * dr
    gh_re = xr * dr + xi * di
    gh_im = xr * di - xi * dr
    q_re = gx_re - gh_im
    q_im = gx_im + gh_re

    stage = contract(jnp.concatenate([q_re, q_im], axis=0), second)
    c2, s2 = stage[:, :inner], stage[:, inner:]
    g_re = c2[:outer] - s2[outer:]
    g_im = c2[outer:] + s2[:outer]
    g_re, g_im = twist(g_re, g_im, 1.0)
    stage = contract(back, jnp.concatenate([g_re, g_im], axis=1))
    c1, s1 = stage[:used], stage[used:]
    in_row = c1[:, :inner] - s1[:, inner:]
    filt_row = c1[:, inner:] + s1[:, :inner]

    cores = lax.axis_size("core")
    pairs = [(index, index ^ 1) for index in range(cores)]
    filt_row = filt_row + lax.ppermute(filt_row, "core", pairs)

    rows_count = lax.axis_size("rows")
    row = lax.axis_index("rows")
    own = (jnp.arange(rows_count) == row)[None, :, None]
    in_blocks = in_row.reshape(seq_count, length_dev)
    filt_blocks = filt_row.reshape(seq_count, length_dev)
    send = jnp.concatenate(
        [
            jnp.where(own, in_blocks[:, None, :], 0.0),
            jnp.broadcast_to(filt_blocks[:, None, :], (seq_count, rows_count, length_dev)),
        ],
        axis=2,
    ).reshape(seq_count * rows_count, 1, 2 * length_dev)
    recv = lax.all_to_all(send, ("seq", "rows"), 0, 0, tiled=True)
    recv = recv.reshape(seq_count, rows_count, 2 * length_dev)
    in_grad = lax.dynamic_index_in_dim(recv[:, :, :length_dev], row, axis=1, keepdims=False)
    parts = recv[:, :, length_dev:]
    filter_grad = parts[:, 0]
    for index in range(1, rows_count):
        filter_grad = filter_grad + parts[:, index]
    return (in_grad.astype(jnp.bfloat16)[None], filter_grad)


def solution(mesh):
    seq_count, batch_count = mesh.devices.shape
    cores = 2
    split = Mesh(
        mesh.devices.reshape(seq_count, batch_count // cores, cores), ("seq", "rows", "core")
    )
    batch = ("rows", "core")
    placed = (P(batch, None, "seq"), P(batch, None, "seq"), P(None, "seq"))
    return jax.shard_map(
        body,
        mesh=split,
        in_specs=placed,
        out_specs=(P(batch, None, "seq"), P(None, "seq")),
        check_vma=False,
    )
```

```python
import numpy as np

import jax
import jax.numpy as jnp
from jax import lax
from jax.sharding import PartitionSpec as P


def contract(left, right):
    return jnp.matmul(
        left, right, precision=lax.Precision.HIGH, preferred_element_type=jnp.float32
    )


def tables(outer, inner, used):
    total = outer * inner
    k1 = np.arange(outer)
    theta1 = 2.0 * np.pi * np.outer(k1, np.arange(used)) / outer
    first = np.concatenate([np.cos(theta1), np.sin(theta1)], axis=0)
    back = np.concatenate([np.cos(theta1).T, np.sin(theta1).T], axis=0) / total
    phi = 2.0 * np.pi * np.outer(k1, np.arange(inner)) / total
    k2 = np.arange(inner)
    theta2 = 2.0 * np.pi * np.outer(k2, k2) / inner
    second = np.concatenate([np.cos(theta2), np.sin(theta2)], axis=1)
    width = second.shape[1]
    pad = lambda a: np.pad(a, ((0, 0), (0, width - a.shape[1])))
    pieces = [second, pad(first), pad(back), pad(np.cos(phi)), pad(np.sin(phi))]
    starts = np.cumsum([0] + [piece.shape[0] for piece in pieces])
    packed = lax.optimization_barrier(jnp.asarray(np.concatenate(pieces).astype(np.float32)))
    cut = lambda i, cols: packed[starts[i] : starts[i + 1], :cols]
    return cut(1, used), cut(2, outer), cut(3, inner), cut(4, inner), cut(0, width)


def body(inputs, out_grad, filters):
    seq_count = lax.axis_size("seq")
    batch_count = lax.axis_size("batch")
    mine = lax.axis_index("batch")
    channels = inputs.shape[1]
    length_dev = inputs.shape[2]
    assert channels == seq_count and inputs.shape[0] == 1
    length = seq_count * length_dev
    total = 2 * length
    inner = 2 * length_dev
    outer = total // inner
    used = length // inner
    first, back, tw_cos, tw_sin, second = tables(outer, inner, used)
    f32 = jnp.float32

    send = jnp.concatenate([inputs[0], out_grad[0]], axis=1).astype(f32)
    send = jnp.concatenate([send, filters], axis=1).reshape(channels, 1, 3 * length_dev)
    recv = lax.all_to_all(send, "seq", 0, 0, tiled=True)
    recv = recv.reshape(seq_count, 3, length_dev)
    signal = recv[:, 0].reshape(used, inner)
    cotangent = recv[:, 1].reshape(used, inner)
    filt = recv[:, 2].reshape(used, inner)

    stage = contract(first, jnp.concatenate([signal, cotangent, filt], axis=1))
    cos_part, sin_part = stage[:outer], stage[outer:]

    def twist(re, im, orient):
        return re * tw_cos - orient * im * tw_sin, im * tw_cos + orient * re * tw_sin

    parts = []
    for index in range(3):
        cut = slice(index * inner, (index + 1) * inner)
        parts.extend(twist(cos_part[:, cut], -sin_part[:, cut], -1.0))

    stage = contract(jnp.concatenate(parts, axis=0), second)
    c2, s2 = stage[:, :inner], stage[:, inner:]
    spectra = []
    for index in range(3):
        re_rows = slice(2 * index * outer, (2 * index + 1) * outer)
        im_rows = slice((2 * index + 1) * outer, (2 * index + 2) * outer)
        spectra.append((c2[re_rows] + s2[im_rows], c2[im_rows] - s2[re_rows]))
    (xr, xi), (dr, di), (hr, hi) = spectra

    gx_re = hr * dr + hi * di
    gx_im = hr * di - hi * dr
    gh_re = xr * dr + xi * di
    gh_im = xr * di - xi * dr
    q_re = gx_re - gh_im
    q_im = gx_im + gh_re

    stage = contract(jnp.concatenate([q_re, q_im], axis=0), second)
    c2, s2 = stage[:, :inner], stage[:, inner:]
    g_re = c2[:outer] - s2[outer:]
    g_im = c2[outer:] + s2[:outer]
    g_re, g_im = twist(g_re, g_im, 1.0)
    stage = contract(back, jnp.concatenate([g_re, g_im], axis=1))
    c1, s1 = stage[:used], stage[used:]
    in_row = c1[:, :inner] - s1[:, inner:]
    filt_row = c1[:, inner:] + s1[:, :inner]

    received = [filt_row]
    for step in range(1, batch_count):
        pairs = [(index, index ^ step) for index in range(batch_count)]
        received.append(lax.ppermute(filt_row, "batch", pairs))
    ordered = []
    for source in range(batch_count):
        pick = received[0]
        for step in range(1, batch_count):
            pick = jnp.where((mine ^ step) == source, received[step], pick)
        ordered.append(pick)
    filt_row = ordered[0]
    for source in range(1, batch_count):
        filt_row = filt_row + ordered[source]

    send = jnp.concatenate(
        [in_row.reshape(seq_count, length_dev), filt_row.reshape(seq_count, length_dev)], axis=1
    )
    recv = lax.all_to_all(send, "seq", 0, 0, tiled=True)
    in_grad = recv[:, :length_dev]
    filter_grad = recv[:, length_dev:]
    return (in_grad.astype(jnp.bfloat16)[None], filter_grad)


def solution(mesh):
    placed = (P("batch", None, "seq"), P("batch", None, "seq"), P(None, "seq"))
    return jax.shard_map(
        body,
        mesh=mesh,
        in_specs=placed,
        out_specs=(P("batch", None, "seq"), P(None, "seq")),
        check_vma=False,
    )
```

```python
import numpy as np

import jax
import jax.numpy as jnp
from jax import lax
from jax.sharding import PartitionSpec as P


def contract(left, right):
    return jnp.matmul(
        left, right, precision=lax.Precision.HIGH, preferred_element_type=jnp.float32
    )


def tables(outer, inner, used):
    total = outer * inner
    k1 = np.arange(outer)
    theta1 = 2.0 * np.pi * np.outer(k1, np.arange(used)) / outer
    first = np.concatenate([np.cos(theta1), np.sin(theta1)], axis=0)
    back = np.concatenate([np.cos(theta1).T, np.sin(theta1).T], axis=0) / total
    phi = 2.0 * np.pi * np.outer(k1, np.arange(inner)) / total
    k2 = np.arange(inner)
    theta2 = 2.0 * np.pi * np.outer(k2, k2) / inner
    second = np.concatenate([np.cos(theta2), np.sin(theta2)], axis=1)
    width = second.shape[1]
    pad = lambda a: np.pad(a, ((0, 0), (0, width - a.shape[1])))
    pieces = [second, pad(first), pad(back), pad(np.cos(phi)), pad(np.sin(phi))]
    starts = np.cumsum([0] + [piece.shape[0] for piece in pieces])
    packed = lax.optimization_barrier(jnp.asarray(np.concatenate(pieces).astype(np.float32)))
    cut = lambda i, cols: packed[starts[i] : starts[i + 1], :cols]
    return cut(1, used), cut(2, outer), cut(3, inner), cut(4, inner), cut(0, width)


def body(inputs, out_grad, filters):
    seq_count = lax.axis_size("seq")
    batch_count = lax.axis_size("batch")
    mine = lax.axis_index("batch")
    channels = inputs.shape[1]
    length_dev = inputs.shape[2]
    assert channels == seq_count and inputs.shape[0] == 1
    length = seq_count * length_dev
    total = 2 * length
    inner = 2 * length_dev
    outer = total // inner
    used = length // inner
    first, back, tw_cos, tw_sin, second = tables(outer, inner, used)
    f32 = jnp.float32

    send = jnp.concatenate([inputs[0], out_grad[0]], axis=1).astype(f32)
    send = jnp.concatenate([send, filters], axis=1).reshape(channels, 1, 3 * length_dev)
    recv = lax.all_to_all(send, "seq", 0, 0, tiled=True)
    recv = recv.reshape(seq_count, 3, length_dev)
    signal = recv[:, 0].reshape(used, inner)
    cotangent = recv[:, 1].reshape(used, inner)
    filt = recv[:, 2].reshape(used, inner)

    stage = contract(first, jnp.concatenate([signal, cotangent, filt], axis=1))
    cos_part, sin_part = stage[:outer], stage[outer:]

    def twist(re, im, orient):
        return re * tw_cos - orient * im * tw_sin, im * tw_cos + orient * re * tw_sin

    parts = []
    for index in range(3):
        cut = slice(index * inner, (index + 1) * inner)
        parts.extend(twist(cos_part[:, cut], -sin_part[:, cut], -1.0))

    stage = contract(jnp.concatenate(parts, axis=0), second)
    c2, s2 = stage[:, :inner], stage[:, inner:]
    spectra = []
    for index in range(3):
        re_rows = slice(2 * index * outer, (2 * index + 1) * outer)
        im_rows = slice((2 * index + 1) * outer, (2 * index + 2) * outer)
        spectra.append((c2[re_rows] + s2[im_rows], c2[im_rows] - s2[re_rows]))
    (xr, xi), (dr, di), (hr, hi) = spectra

    gx_re = hr * dr + hi * di
    gx_im = hr * di - hi * dr
    gh_re = xr * dr + xi * di
    gh_im = xr * di - xi * dr
    q_re = gx_re - gh_im
    q_im = gx_im + gh_re

    stage = contract(jnp.concatenate([q_re, q_im], axis=0), second)
    c2, s2 = stage[:, :inner], stage[:, inner:]
    g_re = c2[:outer] - s2[outer:]
    g_im = c2[outer:] + s2[:outer]
    g_re, g_im = twist(g_re, g_im, 1.0)
    stage = contract(back, jnp.concatenate([g_re, g_im], axis=1))
    c1, s1 = stage[:used], stage[used:]
    in_row = c1[:, :inner] - s1[:, inner:]
    filt_row = c1[:, inner:] + s1[:, :inner]

    received = [filt_row] + [None] * (batch_count - 1)
    for step in reversed(range(1, batch_count)):
        pairs = [(index, index ^ step) for index in range(batch_count)]
        received[step] = lax.ppermute(filt_row, "batch", pairs)
    ordered = []
    for source in range(batch_count):
        pick = received[0]
        for step in range(1, batch_count):
            pick = jnp.where((mine ^ step) == source, received[step], pick)
        ordered.append(pick)
    filt_row = ordered[0]
    for source in range(1, batch_count):
        filt_row = filt_row + ordered[source]

    send = jnp.concatenate(
        [in_row.reshape(seq_count, length_dev), filt_row.reshape(seq_count, length_dev)], axis=1
    )
    recv = lax.all_to_all(send, "seq", 0, 0, tiled=True)
    in_grad = recv[:, :length_dev]
    filter_grad = recv[:, length_dev:]
    return (in_grad.astype(jnp.bfloat16)[None], filter_grad)


def solution(mesh):
    placed = (P("batch", None, "seq"), P("batch", None, "seq"), P(None, "seq"))
    return jax.shard_map(
        body,
        mesh=mesh,
        in_specs=placed,
        out_specs=(P("batch", None, "seq"), P(None, "seq")),
        check_vma=False,
    )
```

```python
import numpy as np

import jax
import jax.numpy as jnp
from jax import lax
from jax.sharding import PartitionSpec as P


def contract(left, right):
    return jnp.matmul(
        left, right, precision=lax.Precision.HIGH, preferred_element_type=jnp.float32
    )


def tables(outer, inner, used):
    total = outer * inner
    k1 = np.arange(outer)
    theta1 = 2.0 * np.pi * np.outer(k1, np.arange(used)) / outer
    first = np.concatenate([np.cos(theta1), np.sin(theta1)], axis=0)
    back = np.concatenate([np.cos(theta1).T, np.sin(theta1).T], axis=0) / total
    phi = 2.0 * np.pi * np.outer(k1, np.arange(inner)) / total
    k2 = np.arange(inner)
    theta2 = 2.0 * np.pi * np.outer(k2, k2) / inner
    second = np.concatenate([np.cos(theta2), np.sin(theta2)], axis=1)
    width = second.shape[1]
    pad = lambda a: np.pad(a, ((0, 0), (0, width - a.shape[1])))
    pieces = [second, pad(first), pad(back), pad(np.cos(phi)), pad(np.sin(phi))]
    starts = np.cumsum([0] + [piece.shape[0] for piece in pieces])
    packed = lax.optimization_barrier(jnp.asarray(np.concatenate(pieces).astype(np.float32)))
    cut = lambda i, cols: packed[starts[i] : starts[i + 1], :cols]
    return cut(1, used), cut(2, outer), cut(3, inner), cut(4, inner), cut(0, width)


def body(inputs, out_grad, filters):
    seq_count = lax.axis_size("seq")
    batch_count = lax.axis_size("batch")
    mine = lax.axis_index("batch")
    channels = inputs.shape[1]
    length_dev = inputs.shape[2]
    assert channels == seq_count and inputs.shape[0] == 1
    length = seq_count * length_dev
    total = 2 * length
    inner = 2 * length_dev
    outer = total // inner
    used = length // inner
    first, back, tw_cos, tw_sin, second = tables(outer, inner, used)
    f32 = jnp.float32

    send = jnp.concatenate([inputs[0], out_grad[0]], axis=1).astype(f32)
    send = jnp.concatenate([send, filters], axis=1).reshape(channels, 1, 3 * length_dev)
    recv = lax.all_to_all(send, "seq", 0, 0, tiled=True)
    recv = recv.reshape(seq_count, 3, length_dev)
    signal = recv[:, 0].reshape(used, inner)
    cotangent = recv[:, 1].reshape(used, inner)
    filt = recv[:, 2].reshape(used, inner)

    partner = lax.ppermute(
        jnp.stack([signal, cotangent]), "batch", [(i, i ^ 1) for i in range(batch_count)]
    )
    odd = (mine & 1) == 1
    sig_lo = jnp.where(odd, partner[0], signal)
    cot_lo = jnp.where(odd, partner[1], cotangent)
    sig_hi = jnp.where(odd, signal, partner[0])
    cot_hi = jnp.where(odd, cotangent, partner[1])
    rows = [sig_lo, cot_lo, sig_hi, cot_hi, filt]

    stage = contract(first, jnp.concatenate(rows, axis=1))
    cos_part, sin_part = stage[:outer], stage[outer:]

    def twist(re, im, orient):
        return re * tw_cos - orient * im * tw_sin, im * tw_cos + orient * re * tw_sin

    parts = []
    for index in range(len(rows)):
        cut = slice(index * inner, (index + 1) * inner)
        parts.extend(twist(cos_part[:, cut], -sin_part[:, cut], -1.0))

    stage = contract(jnp.concatenate(parts, axis=0), second)
    c2, s2 = stage[:, :inner], stage[:, inner:]
    spectra = []
    for index in range(len(rows)):
        re_rows = slice(2 * index * outer, (2 * index + 1) * outer)
        im_rows = slice((2 * index + 1) * outer, (2 * index + 2) * outer)
        spectra.append((c2[re_rows] + s2[im_rows], c2[im_rows] - s2[re_rows]))
    (xlr, xli), (dlr, dli), (xhr, xhi), (dhr, dhi), (hr, hi) = spectra
    dr = jnp.where(odd, dhr, dlr)
    di = jnp.where(odd, dhi, dli)

    gx_re = hr * dr + hi * di
    gx_im = hr * di - hi * dr
    gh_re = (xlr * dlr + xli * dli) + (xhr * dhr + xhi * dhi)
    gh_im = (xlr * dli - xli * dlr) + (xhr * dhi - xhi * dhr)

    stage = contract(jnp.concatenate([gx_re, gx_im, gh_re, gh_im], axis=0), second)
    c2, s2 = stage[:, :inner], stage[:, inner:]
    grads = []
    for index in range(2):
        re_rows = slice(2 * index * outer, (2 * index + 1) * outer)
        im_rows = slice((2 * index + 1) * outer, (2 * index + 2) * outer)
        grads.extend(twist(c2[re_rows] - s2[im_rows], c2[im_rows] + s2[re_rows], 1.0))
    stage = contract(back, jnp.concatenate(grads, axis=1))
    c1, s1 = stage[:used], stage[used:]
    in_row = c1[:, :inner] - s1[:, inner : 2 * inner]
    filt_row = c1[:, 2 * inner : 3 * inner] - s1[:, 3 * inner :]

    filt_row = filt_row + lax.ppermute(
        filt_row, "batch", [(i, i ^ 2) for i in range(batch_count)]
    )

    send = jnp.concatenate(
        [in_row.reshape(seq_count, length_dev), filt_row.reshape(seq_count, length_dev)], axis=1
    )
    recv = lax.all_to_all(send, "seq", 0, 0, tiled=True)
    in_grad = recv[:, :length_dev]
    filter_grad = recv[:, length_dev:]
    return (in_grad.astype(jnp.bfloat16)[None], filter_grad)


def solution(mesh):
    placed = (P("batch", None, "seq"), P("batch", None, "seq"), P(None, "seq"))
    return jax.shard_map(
        body,
        mesh=mesh,
        in_specs=placed,
        out_specs=(P("batch", None, "seq"), P(None, "seq")),
        check_vma=False,
    )
```

```python
import numpy as np

import jax
import jax.numpy as jnp
from jax import lax
from jax.sharding import PartitionSpec as P


def contract(left, right):
    return jnp.matmul(
        left, right, precision=lax.Precision.HIGH, preferred_element_type=jnp.float32
    )


def tables(outer, inner, used):
    total = outer * inner
    k1 = np.arange(outer)
    theta1 = 2.0 * np.pi * np.outer(k1, np.arange(used)) / outer
    first = np.concatenate([np.cos(theta1), np.sin(theta1)], axis=0)
    back = np.concatenate([np.cos(theta1).T, np.sin(theta1).T], axis=0) / total
    phi = 2.0 * np.pi * np.outer(k1, np.arange(inner)) / total
    k2 = np.arange(inner)
    theta2 = 2.0 * np.pi * np.outer(k2, k2) / inner
    second = np.concatenate([np.cos(theta2), np.sin(theta2)], axis=1)
    width = second.shape[1]
    pad = lambda a: np.pad(a, ((0, 0), (0, width - a.shape[1])))
    pieces = [second, pad(first), pad(back), pad(np.cos(phi)), pad(np.sin(phi))]
    starts = np.cumsum([0] + [piece.shape[0] for piece in pieces])
    packed = lax.optimization_barrier(jnp.asarray(np.concatenate(pieces).astype(np.float32)))
    cut = lambda i, cols: packed[starts[i] : starts[i + 1], :cols]
    return cut(1, used), cut(2, outer), cut(3, inner), cut(4, inner), cut(0, width)


def body(inputs, out_grad, filters):
    seq_count = lax.axis_size("seq")
    batch_count = lax.axis_size("batch")
    mine = lax.axis_index("batch")
    channels = inputs.shape[1]
    length_dev = inputs.shape[2]
    assert channels == seq_count and inputs.shape[0] == 1
    length = seq_count * length_dev
    total = 2 * length
    inner = 2 * length_dev
    outer = total // inner
    used = length // inner
    first, back, tw_cos, tw_sin, second = tables(outer, inner, used)
    f32 = jnp.float32

    send = jnp.concatenate([inputs[0], out_grad[0]], axis=1).astype(f32)
    send = jnp.concatenate([send, filters], axis=1).reshape(channels, 1, 3 * length_dev)
    recv = lax.all_to_all(send, "seq", 0, 0, tiled=True)
    recv = recv.reshape(seq_count, 3, length_dev)
    signal = recv[:, 0].reshape(used, inner)
    cotangent = recv[:, 1].reshape(used, inner)
    filt = recv[:, 2].reshape(used, inner)

    partner = lax.ppermute(
        jnp.stack([signal, cotangent]), "batch", [(i, i ^ 1) for i in range(batch_count)]
    )
    odd = (mine & 1) == 1
    sig_lo = jnp.where(odd, partner[0], signal)
    cot_lo = jnp.where(odd, partner[1], cotangent)
    sig_hi = jnp.where(odd, signal, partner[0])
    cot_hi = jnp.where(odd, cotangent, partner[1])
    rows = [sig_lo, cot_lo, sig_hi, cot_hi, filt]

    stage = contract(first, jnp.concatenate(rows, axis=1))
    cos_part, sin_part = stage[:outer], stage[outer:]

    def twist(re, im, orient):
        return re * tw_cos - orient * im * tw_sin, im * tw_cos + orient * re * tw_sin

    parts = []
    for index in range(len(rows)):
        cut = slice(index * inner, (index + 1) * inner)
        parts.extend(twist(cos_part[:, cut], -sin_part[:, cut], -1.0))

    stage = contract(jnp.concatenate(parts, axis=0), second)
    c2, s2 = stage[:, :inner], stage[:, inner:]
    spectra = []
    for index in range(len(rows)):
        re_rows = slice(2 * index * outer, (2 * index + 1) * outer)
        im_rows = slice((2 * index + 1) * outer, (2 * index + 2) * outer)
        spectra.append((c2[re_rows] + s2[im_rows], c2[im_rows] - s2[re_rows]))
    (xlr, xli), (dlr, dli), (xhr, xhi), (dhr, dhi), (hr, hi) = spectra
    dr = jnp.where(odd, dhr, dlr)
    di = jnp.where(odd, dhi, dli)

    gx_re = hr * dr + hi * di
    gx_im = hr * di - hi * dr
    gh_re = (xlr * dlr + xli * dli) + (xhr * dhr + xhi * dhi)
    gh_im = (xlr * dli - xli * dlr) + (xhr * dhi - xhi * dhr)

    def inverse(re, im):
        stage = contract(jnp.concatenate([re, im], axis=0), second)
        c2, s2 = stage[:, :inner], stage[:, inner:]
        g_re, g_im = twist(c2[:outer] - s2[outer:], c2[outer:] + s2[:outer], 1.0)
        stage = contract(back, jnp.concatenate([g_re, g_im], axis=1))
        return stage[:used, :inner] - stage[used:, inner:]

    filt_row = inverse(gh_re, gh_im)
    filt_row, gx_re, gx_im = lax.optimization_barrier((filt_row, gx_re, gx_im))
    other = lax.ppermute(filt_row, "batch", [(i, i ^ 2) for i in range(batch_count)])
    in_row = inverse(gx_re, gx_im)
    filt_row = filt_row + other

    send = jnp.concatenate(
        [in_row.reshape(seq_count, length_dev), filt_row.reshape(seq_count, length_dev)], axis=1
    )
    recv = lax.all_to_all(send, "seq", 0, 0, tiled=True)
    in_grad = recv[:, :length_dev]
    filter_grad = recv[:, length_dev:]
    return (in_grad.astype(jnp.bfloat16)[None], filter_grad)


def solution(mesh):
    placed = (P("batch", None, "seq"), P("batch", None, "seq"), P(None, "seq"))
    return jax.shard_map(
        body,
        mesh=mesh,
        in_specs=placed,
        out_specs=(P("batch", None, "seq"), P(None, "seq")),
        check_vma=False,
    )
```

```python
import numpy as np

import jax
import jax.numpy as jnp
from jax import lax
from jax.sharding import PartitionSpec as P


def contract(left, right):
    return jnp.matmul(
        left, right, precision=lax.Precision.HIGH, preferred_element_type=jnp.float32
    )


def tables(outer, inner, used):
    total = outer * inner
    k1 = np.arange(outer)
    theta1 = 2.0 * np.pi * np.outer(k1, np.arange(used)) / outer
    first = np.concatenate([np.cos(theta1), np.sin(theta1)], axis=0)
    back = np.concatenate([np.cos(theta1).T, np.sin(theta1).T], axis=0) / total
    phi = 2.0 * np.pi * np.outer(k1, np.arange(inner)) / total
    k2 = np.arange(inner)
    theta2 = 2.0 * np.pi * np.outer(k2, k2) / inner
    second = np.concatenate([np.cos(theta2), np.sin(theta2)], axis=1)
    width = second.shape[1]
    pad = lambda a: np.pad(a, ((0, 0), (0, width - a.shape[1])))
    pieces = [second, pad(first), pad(back), pad(np.cos(phi)), pad(np.sin(phi))]
    starts = np.cumsum([0] + [piece.shape[0] for piece in pieces])
    packed = lax.optimization_barrier(jnp.asarray(np.concatenate(pieces).astype(np.float32)))
    cut = lambda i, cols: packed[starts[i] : starts[i + 1], :cols]
    return cut(1, used), cut(2, outer), cut(3, inner), cut(4, inner), cut(0, width)


def body(inputs, out_grad, filters):
    seq_count = lax.axis_size("seq")
    batch_count = lax.axis_size("batch")
    mine = lax.axis_index("batch")
    channels = inputs.shape[1]
    length_dev = inputs.shape[2]
    assert channels == seq_count and inputs.shape[0] == 1
    length = seq_count * length_dev
    total = 2 * length
    inner = 2 * length_dev
    outer = total // inner
    used = length // inner
    first, back, tw_cos, tw_sin, second = tables(outer, inner, used)
    f32 = jnp.float32

    send = jnp.concatenate([inputs[0], out_grad[0]], axis=1).astype(f32)
    send = jnp.concatenate([send, filters], axis=1).reshape(channels, 1, 3 * length_dev)
    recv = lax.all_to_all(send, "seq", 0, 0, tiled=True)
    recv = recv.reshape(seq_count, 3, length_dev)
    signal = recv[:, 0].reshape(used, inner)
    cotangent = recv[:, 1].reshape(used, inner)
    filt = recv[:, 2].reshape(used, inner)

    partner = lax.ppermute(
        jnp.stack([signal, cotangent]), "batch", [(i, i ^ 1) for i in range(batch_count)]
    )
    odd = (mine & 1) == 1

    def twist(re, im, orient):
        return re * tw_cos - orient * im * tw_sin, im * tw_cos + orient * re * tw_sin

    def forward(rows):
        stage = contract(first, jnp.concatenate(rows, axis=1))
        cos_part, sin_part = stage[:outer], stage[outer:]
        parts = []
        for index in range(len(rows)):
            cut = slice(index * inner, (index + 1) * inner)
            parts.extend(twist(cos_part[:, cut], -sin_part[:, cut], -1.0))
        stage = contract(jnp.concatenate(parts, axis=0), second)
        c2, s2 = stage[:, :inner], stage[:, inner:]
        spectra = []
        for index in range(len(rows)):
            re_rows = slice(2 * index * outer, (2 * index + 1) * outer)
            im_rows = slice((2 * index + 1) * outer, (2 * index + 2) * outer)
            spectra.append((c2[re_rows] + s2[im_rows], c2[im_rows] - s2[re_rows]))
        return spectra

    own = forward([signal, cotangent, filt])
    other = forward([partner[0], partner[1], filt])
    pick = lambda a, b: tuple(jnp.where(odd, v, u) for u, v in zip(a, b))
    (xlr, xli), (dlr, dli) = pick(own[0], other[0]), pick(own[1], other[1])
    (xhr, xhi), (dhr, dhi) = pick(other[0], own[0]), pick(other[1], own[1])
    hr, hi = own[2]
    dr, di = own[1]

    gx_re = hr * dr + hi * di
    gx_im = hr * di - hi * dr
    gh_re = (xlr * dlr + xli * dli) + (xhr * dhr + xhi * dhi)
    gh_im = (xlr * dli - xli * dlr) + (xhr * dhi - xhi * dhr)

    def inverse(re, im):
        stage = contract(jnp.concatenate([re, im], axis=0), second)
        c2, s2 = stage[:, :inner], stage[:, inner:]
        g_re, g_im = twist(c2[:outer] - s2[outer:], c2[outer:] + s2[:outer], 1.0)
        stage = contract(back, jnp.concatenate([g_re, g_im], axis=1))
        return stage[:used, :inner] - stage[used:, inner:]

    filt_row = inverse(gh_re, gh_im)
    filt_row, gx_re, gx_im = lax.optimization_barrier((filt_row, gx_re, gx_im))
    other = lax.ppermute(filt_row, "batch", [(i, i ^ 2) for i in range(batch_count)])
    in_row = inverse(gx_re, gx_im)
    filt_row = filt_row + other

    send = jnp.concatenate(
        [in_row.reshape(seq_count, length_dev), filt_row.reshape(seq_count, length_dev)], axis=1
    )
    recv = lax.all_to_all(send, "seq", 0, 0, tiled=True)
    in_grad = recv[:, :length_dev]
    filter_grad = recv[:, length_dev:]
    return (in_grad.astype(jnp.bfloat16)[None], filter_grad)


def solution(mesh):
    placed = (P("batch", None, "seq"), P("batch", None, "seq"), P(None, "seq"))
    return jax.shard_map(
        body,
        mesh=mesh,
        in_specs=placed,
        out_specs=(P("batch", None, "seq"), P(None, "seq")),
        check_vma=False,
    )
```
